512 devices in a mesh: dp: 16 (over z), expert: 32 (over y, x, core).
Axes of the slice: x: 4, y: 4, z: 16, core: 2. Of those that a mesh axis runs over, the one named last changes fastest.
Arguments:
- tokens: bfloat16 [65536, 1024], P(('dp', 'expert')), may hold values from -24 to 24
- expert_ids: int32 [65536, 2], P(('dp', 'expert')), may hold values from 0 to 31, all different within a row; in each aligned block of 128 rows (0 to 127, 128 to 255, ...) at most 32 rows name the same one
- route_probs: float32 [65536, 2], P(('dp', 'expert')), may hold values from 0.1 to 1
- w_gate: bfloat16 [32, 1024, 384], P('expert', 'dp'), may hold values from -0.1875 to 0.1875
- w_up: bfloat16 [32, 1024, 384], P('expert', 'dp'), may hold values from -0.1875 to 0.1875
- w_down: bfloat16 [32, 384, 1024], P('expert', None, 'dp'), may hold values from -0.3125 to 0.3125
- grad_out: bfloat16 [65536, 1024], P(('dp', 'expert')), may hold values from -2.5 to 2.5
Outputs:
- mixed_out: bfloat16 [65536, 1024], P(('dp', 'expert'))
- grad_tokens: bfloat16 [65536, 1024], P(('dp', 'expert'))
- grad_probs: float32 [65536, 2], P(('dp', 'expert'))
- grad_w_gate: bfloat16 [32, 1024, 384], P('expert', 'dp')
- grad_w_up: bfloat16 [32, 1024, 384], P('expert', 'dp')
- grad_w_down: bfloat16 [32, 384, 1024], P('expert', None, 'dp')
The draws below stay inside these ranges and needn't reach their ends.
Inputs may be any that keep to these rules, and one draw needn't show every extreme that they name: `expert_ids`: each row names 2 different experts. Within the rows of one device no expert is named by more than 32 rows, and in every draw some expert is named by exactly 32 rows of some device.
All inputs are finite; a program needn't handle non-finite values.
Results may differ from the reference program's by a relative error of at most 0.017.
Values may be sent and summed in bfloat16 or wider, within the bound.
No kernel may reach another device: no remote copies, remote signals or barrier semaphores. Data moves between devices by JAX's collectives and lax.ppermute only.
A program may use at most 128 MiB of HBM per device.

```python
import math
import jax
import jax.numpy as jnp
import numpy as np
from jax import lax

D = 1024
H = 384
TOPK = 2
TOK_DEV = 128
EXPERTS = 32
CAP = 32
TOKENS = 65536
N_DP = 16
N_EXPERT = 32


def strengthened(result, rng, source, target, shards_of, factor):
    owner, partner = [(jnp.arange(result.shape[axis_at]) // (result.shape[axis_at] // shards_of)).reshape([-1 if axis == axis_at else 1 for axis in range(result.ndim)]) for axis_at in (source, target)]
    chosen = jax.random.permutation(rng, shards_of)[partner]
    strong = (owner == chosen) | (owner == (partner + shards_of // 2) % shards_of)
    return jnp.where(strong, factor * result, result)


def block_levels(own_key, dims, cuts, low, top_value):
    loudness, own = 1.0, jax.random.fold_in(own_key, 6)
    for axis_at, parts in cuts:
        heights = jnp.exp(jax.random.uniform(jax.random.fold_in(own, axis_at), (parts,), jnp.float32, low / len(cuts), top_value / len(cuts)))
        loudness = loudness * jnp.repeat(heights, dims[axis_at] // parts).reshape([-1 if axis == axis_at else 1 for axis in range(len(dims))])
    return loudness


def routed_block(stream_key, own, number, rows, count, top, limit, skew):
    ranking = jax.random.permutation(stream_key, count)
    packed, common = portions_of(count, rows * top, limit, skew, True), portions_of(count, rows * top, limit, skew, False)
    places = jnp.arange(count)

    def named(sizes, rotation):
        used = int((sizes > 0).sum())
        fixed = max(1, used // 4)
        passed = fixed + (places - fixed + rotation * (used - fixed)) % max(1, count - fixed)
        return jnp.zeros((count,), jnp.int32).at[ranking[jnp.where(places < fixed, places, passed)]].set(jnp.asarray(sizes, jnp.int32))

    sizes = jnp.where(number % 4 == 0, named(packed, number // 4), named(common, number - number // 4 - 1))
    mixed = jax.random.permutation(jax.random.fold_in(own, 3), count)
    giver, sink = mixed[0:count // 2 * 2:2], mixed[1:count // 2 * 2:2]
    slack = jnp.minimum(sizes[giver] - 1, limit - sizes[sink]) // 2
    slack = jnp.where((giver == ranking[0]) | (sink == ranking[0]) | (sizes[sink] == 0), 0, jnp.maximum(slack, 0))
    passed = jax.random.randint(jax.random.fold_in(own, 4), (count // 2,), 0, 1 << 20) % (slack + 1)
    sizes = sizes.at[giver].add(-passed).at[sink].add(passed)
    members = jnp.searchsorted(jnp.cumsum(sizes), jnp.arange(rows * top), side="right").astype(jnp.int32)
    grid = members.reshape(top, rows).T
    grid = grid[jax.random.permutation(jax.random.fold_in(own, 1), rows)]
    rotation = jax.random.randint(jax.random.fold_in(own, 2), (rows, 1), 0, top)
    return jnp.take_along_axis(grid, (jnp.arange(top)[None, :] + rotation) % top, axis=1)


def portions_of(amount, total, bound, skew, full):
    loads = [(1 << 20) // math.isqrt(grade ** skew) + 1 for grade in range(1, amount + 1)]
    largest = bound if full else min(bound, max(-(-total // amount), total * loads[0] // sum(loads)))
    least = 1 if total - largest >= amount - 1 else 0
    given, spare = [largest] + [least] * (amount - 1), total - largest - least * (amount - 1)
    while spare > 0:
        candidates = [i for i in range(1, amount) if given[i] < largest] or [i for i in range(1, amount) if given[i] < bound]
        mass, budget = sum([loads[i] for i in candidates]), spare
        for i in candidates:
            addition = min(bound - given[i], max(1, budget * loads[i] // mass), spare)
            given[i] = given[i] + addition
            spare = spare - addition
    return np.array(given)


def normal_values(own_key, shape, width, most, pieces=(), kind=jnp.bfloat16):
    gain = block_levels(own_key, shape, pieces, -0.22, 0.18) if pieces else 1.0
    entries = jax.random.normal(own_key, shape, jnp.float32) * width * gain
    return jnp.minimum(jnp.maximum(entries, -most), most).astype(kind)


def bell_draw_with(own_key, shape, spread, bound, split, heavy, held_as=jnp.bfloat16):
    drawn = spread * jax.random.normal(own_key, shape, jnp.float32)
    if split:
        drawn = drawn * block_levels(own_key, shape, split, -0.22, 0.18)
    return jnp.clip(strengthened(drawn, jax.random.fold_in(own_key, 3), *heavy), -bound, bound).astype(held_as)


def setup_inputs(seed: int = 0) -> dict:
    key_of = jax.random.split(jax.random.key(seed), 8)
    tokens = bell_draw_with(key_of[0], (TOKENS, D), 1.0, 24.0, ((0, 512),), (0, 1, 512, 6.0))
    expert_ids_keys = jax.random.split(jax.random.fold_in(key_of[1], 1), TOKENS // TOK_DEV)
    expert_ids_turns = jax.random.permutation(jax.random.fold_in(key_of[1], 3), TOKENS // TOK_DEV)
    expert_ids = jax.vmap(lambda own, number: routed_block(jax.random.fold_in(key_of[1], 2), own, number, TOK_DEV, EXPERTS, TOPK, CAP, 1))(expert_ids_keys, expert_ids_turns).reshape((TOKENS, TOPK))
    route_probs = jnp.clip(0.1 + 0.9 * jax.random.uniform(key_of[2], (TOKENS, TOPK), jnp.float32) ** block_levels(key_of[2], (TOKENS, TOPK), ((0, 512),), -0.2, 0.2), 0.1, 1.0)
    w_gate = normal_values(key_of[3], (EXPERTS, D, H), D ** -0.5, 0.1875, ((0, 32), (1, 16)))
    w_up = normal_values(key_of[4], (EXPERTS, D, H), D ** -0.5, 0.1875, ((0, 32), (1, 16)))
    w_down = normal_values(key_of[5], (EXPERTS, H, D), H ** -0.5, 0.3125, ((0, 32), (2, 16)))
    grad_out = normal_values(key_of[6], (TOKENS, D), 0.25, 2.5, ((0, 512),))
    return dict(tokens=tokens, expert_ids=expert_ids, route_probs=route_probs, w_gate=w_gate, w_up=w_up, w_down=w_down, grad_out=grad_out)


def route_slots(expert_ids, experts):
    flat_ids = expert_ids.reshape(-1)
    onehot = (flat_ids[:, None] == jnp.arange(experts, dtype=jnp.int32)[None, :]).astype(jnp.int32)
    before = jnp.cumsum(onehot, axis=0) - onehot
    slot_of = jnp.sum(before * onehot, axis=1).astype(jnp.int32)
    return flat_ids.astype(jnp.int32), slot_of


def contract_rows(left_op, right_op):
    return lax.dot_general(left_op, right_op, (((0,), (0,)), ((), ())), preferred_element_type=jnp.float32)


def contract_cols(left_op, right_op):
    return lax.dot_general(left_op, right_op, (((1,), (1,)), ((), ())), preferred_element_type=jnp.float32)


def group_sum(left_op, right_op):
    left_g = left_op.reshape(N_DP, N_EXPERT * CAP, -1).astype(jnp.float32)
    right_g = right_op.reshape(N_DP, N_EXPERT * CAP, -1).astype(jnp.float32)
    group_terms = jnp.einsum("grd,grh->gdh", left_g, right_g, precision=lax.Precision.HIGHEST).astype(jnp.bfloat16)
    group_terms = lax.optimization_barrier(group_terms)
    return jnp.sum(group_terms.astype(jnp.float32), axis=0).astype(jnp.bfloat16)


def reference(tokens, expert_ids, route_probs, w_gate, w_up, w_down, grad_out):
    sources = N_DP * N_EXPERT
    assigned = TOK_DEV * TOPK
    tok_blocks = tokens.reshape(sources, TOK_DEV, D)
    grad_blocks = grad_out.reshape(sources, TOK_DEV, D)
    prob_blocks = route_probs.reshape(sources, assigned)
    flat_ids, slot_of = jax.vmap(lambda id_block: route_slots(id_block, EXPERTS))(expert_ids.reshape(sources, TOK_DEV, TOPK))
    assign = jnp.broadcast_to(jnp.arange(assigned, dtype=jnp.int32)[None, :], (sources, assigned))
    source_of = jnp.broadcast_to(jnp.arange(sources, dtype=jnp.int32)[:, None], (sources, assigned))
    inverse = jnp.full((sources, EXPERTS, CAP), -1, jnp.int32).at[source_of, flat_ids, slot_of].set(assign)
    pick_rows = jax.vmap(lambda table_rows, where_from: table_rows[where_from])
    add_rows = jax.vmap(lambda running, where_to, values: running.at[where_to].add(values, mode="drop"))
    set_vals = jax.vmap(lambda running, where_to, values: running.at[where_to].set(values, mode="drop"))

    def per_expert(carried, expert):
        mixed_run, back_run, prob_run = carried
        slot_table = lax.dynamic_index_in_dim(inverse, expert, axis=1, keepdims=False)
        filled = slot_table >= 0
        assign_c = jnp.maximum(slot_table, 0).astype(jnp.int32)
        tok_index = (assign_c // TOPK).astype(jnp.int32)
        zero_rows = jnp.zeros((sources, CAP, D), jnp.bfloat16)
        slot_rows = jnp.where(filled[:, :, None], pick_rows(tok_blocks, tok_index), zero_rows)
        probs_here = jnp.take_along_axis(prob_blocks, assign_c, axis=1)
        grad_raw = pick_rows(grad_blocks, tok_index).astype(jnp.float32)
        scaled = (probs_here[:, :, None] * grad_raw).astype(jnp.bfloat16)
        grad_rows = jnp.where(filled[:, :, None], scaled, zero_rows)
        gate_mat = lax.dynamic_index_in_dim(w_gate, expert, 0, keepdims=False)
        up_mat = lax.dynamic_index_in_dim(w_up, expert, 0, keepdims=False)
        down_mat = lax.dynamic_index_in_dim(w_down, expert, 0, keepdims=False)
        flat_rows = slot_rows.reshape(sources * CAP, D)
        flat_grad = grad_rows.reshape(sources * CAP, D)
        gate_pre = jnp.dot(flat_rows, gate_mat, preferred_element_type=jnp.float32)
        up_pre = jnp.dot(flat_rows, up_mat, preferred_element_type=jnp.float32)
        sigmoid_g = jax.nn.sigmoid(gate_pre)
        activated = gate_pre * sigmoid_g
        hidden = (activated * up_pre).astype(jnp.bfloat16)
        expert_out = jnp.dot(hidden, down_mat, preferred_element_type=jnp.float32).astype(jnp.bfloat16)
        back_hidden = contract_cols(flat_grad, down_mat)
        back_gate = (back_hidden * up_pre * sigmoid_g * (1.0 + gate_pre * (1.0 - sigmoid_g))).astype(jnp.bfloat16)
        back_up = (back_hidden * activated).astype(jnp.bfloat16)
        back_rows = (contract_cols(back_gate, gate_mat) + contract_cols(back_up, up_mat)).astype(jnp.bfloat16)
        grad_gate = group_sum(flat_rows, back_gate)
        grad_up = group_sum(flat_rows, back_up)
        grad_down = group_sum(hidden, flat_grad)
        out_f = expert_out.reshape(sources, CAP, D).astype(jnp.float32)
        tok_target = jnp.where(filled, tok_index, TOK_DEV).astype(jnp.int32)
        mixed_run = add_rows(mixed_run, tok_target, probs_here[:, :, None] * out_f)
        back_run = add_rows(back_run, tok_target, back_rows.reshape(sources, CAP, D).astype(jnp.float32))
        prob_vals = jnp.sum(grad_raw * out_f, axis=2)
        assign_target = jnp.where(filled, assign_c, assigned).astype(jnp.int32)
        prob_run = set_vals(prob_run, assign_target, prob_vals)
        return (mixed_run, back_run, prob_run), (grad_gate, grad_up, grad_down)

    initial = (jnp.zeros((sources, TOK_DEV, D), jnp.float32), jnp.zeros((sources, TOK_DEV, D), jnp.float32), jnp.zeros((sources, assigned), jnp.float32))
    finals, grads = lax.scan(per_expert, initial, jnp.arange(EXPERTS, dtype=jnp.int32))
    mixed_out = finals[0].reshape(TOKENS, D).astype(jnp.bfloat16)
    grad_tokens = finals[1].reshape(TOKENS, D).astype(jnp.bfloat16)
    grad_probs = finals[2].reshape(TOKENS, TOPK)
    return (mixed_out, grad_tokens, grad_probs, grads[0], grads[1], grads[2])
```

```python
import jax
import jax.numpy as jnp
from jax import lax
from jax.sharding import PartitionSpec as P


def route_slots(expert_ids, experts):
    flat_ids = expert_ids.reshape(-1)
    onehot = (flat_ids[:, None] == jnp.arange(experts, dtype=jnp.int32)[None, :]).astype(jnp.int32)
    before = jnp.cumsum(onehot, axis=0) - onehot
    slot_of = jnp.sum(before * onehot, axis=1)
    return flat_ids, slot_of


def contract_rows(left_op, right_op):
    return lax.dot_general(
        left_op, right_op, (((0,), (0,)), ((), ())), preferred_element_type=jnp.float32
    )


def contract_cols(left_op, right_op):
    return lax.dot_general(
        left_op, right_op, (((1,), (1,)), ((), ())), preferred_element_type=jnp.float32
    )


def shards(tokens, expert_ids, route_probs, w_gate, w_up, w_down, grad_out):
    senders = lax.axis_size("expert")
    tok_rows, model_width = tokens.shape
    top_count = expert_ids.shape[1]
    hidden_width = w_gate.shape[2]
    capacity = min(tok_rows, 4 * tok_rows * top_count // senders)
    total_rows = senders * capacity
    flat_ids, slot_of = route_slots(expert_ids, senders)
    token_of = jnp.arange(tok_rows * top_count, dtype=jnp.int32) // top_count

    packed = jnp.concatenate([w_gate[0], w_up[0], w_down[0].T], axis=1)
    whole = lax.all_gather(packed, "dp", axis=0, tiled=True)
    gate_up = whole[:, : 2 * hidden_width]
    down_t = whole[:, 2 * hidden_width :]

    grad_wide = grad_out.astype(jnp.float32)
    scaled = (
        (route_probs[:, :, None] * grad_wide[:, None, :])
        .astype(jnp.bfloat16)
        .reshape(tok_rows * top_count, model_width)
    )
    base = flat_ids * (2 * capacity) + slot_of
    places = jnp.concatenate([base, base + capacity])
    values = jnp.concatenate([tokens[token_of], scaled], axis=0)
    outgoing = jnp.zeros((2 * total_rows, model_width), jnp.bfloat16).at[places].set(values)
    arrived = lax.all_to_all(
        outgoing.reshape(senders, 2 * capacity, model_width),
        "expert",
        split_axis=0,
        concat_axis=0,
        tiled=True,
    )
    slot_rows = arrived[:, :capacity].reshape(total_rows, model_width)
    grad_in = arrived[:, capacity:].reshape(total_rows, model_width)

    both_pre = jnp.dot(slot_rows, gate_up, preferred_element_type=jnp.float32)
    gate_pre = both_pre[:, :hidden_width]
    up_pre = both_pre[:, hidden_width:]
    sigmoid_g = jax.nn.sigmoid(gate_pre)
    activated = gate_pre * sigmoid_g
    hidden = (activated * up_pre).astype(jnp.bfloat16)
    back_hidden = jnp.dot(grad_in, down_t, preferred_element_type=jnp.float32)
    back_gate = (back_hidden * up_pre * sigmoid_g * (1.0 + gate_pre * (1.0 - sigmoid_g))).astype(
        jnp.bfloat16
    )
    back_up = (back_hidden * activated).astype(jnp.bfloat16)
    back_both = jnp.concatenate([back_gate, back_up], axis=1)

    grad_terms = jnp.concatenate(
        [
            contract_rows(slot_rows, back_both).astype(jnp.bfloat16),
            contract_rows(grad_in, hidden).astype(jnp.bfloat16),
        ],
        axis=1,
    )
    summed = lax.psum_scatter(grad_terms, "dp", scatter_dimension=0, tiled=True)

    expert_out = contract_cols(hidden, down_t).astype(jnp.bfloat16)
    returned = lax.all_to_all(
        expert_out.reshape(senders, capacity, model_width),
        "expert",
        split_axis=0,
        concat_axis=0,
        tiled=True,
    )
    back_rows = contract_cols(back_both, gate_up).astype(jnp.bfloat16)
    sent_back = lax.all_to_all(
        back_rows.reshape(senders, capacity, model_width),
        "expert",
        split_axis=0,
        concat_axis=0,
        tiled=True,
    )

    slot_place = flat_ids * capacity + slot_of
    picked = (
        returned.reshape(total_rows, model_width)[slot_place]
        .reshape(tok_rows, top_count, model_width)
        .astype(jnp.float32)
    )
    mixed_out = jnp.sum(route_probs[:, :, None] * picked, axis=1).astype(jnp.bfloat16)
    grad_probs = jnp.sum(grad_wide[:, None, :] * picked, axis=2)
    back_picked = sent_back.reshape(total_rows, model_width)[slot_place].reshape(
        tok_rows, top_count, model_width
    )
    grad_tokens = jnp.sum(back_picked.astype(jnp.float32), axis=1).astype(jnp.bfloat16)

    summed = summed.astype(jnp.float32).astype(jnp.bfloat16)
    grad_w_gate = summed[:, :hidden_width][None]
    grad_w_up = summed[:, hidden_width : 2 * hidden_width][None]
    grad_w_down = summed[:, 2 * hidden_width :].T[None]
    return (mixed_out, grad_tokens, grad_probs, grad_w_gate, grad_w_up, grad_w_down)


def solution(mesh):
    placed = (
        P(("dp", "expert"), None),
        P(("dp", "expert"), None),
        P(("dp", "expert"), None),
        P("expert", "dp", None),
        P("expert", "dp", None),
        P("expert", None, "dp"),
        P(("dp", "expert"), None),
    )
    return jax.shard_map(
        shards,
        mesh=mesh,
        in_specs=placed,
        out_specs=(
            P(("dp", "expert"), None),
            P(("dp", "expert"), None),
            P(("dp", "expert"), None),
            P("expert", "dp", None),
            P("expert", "dp", None),
            P("expert", None, "dp"),
        ),
        check_vma=False,
    )
```

```python
import jax
import jax.numpy as jnp
from jax import lax
from jax.sharding import PartitionSpec as P


def route_slots(expert_ids, experts):
    flat_ids = expert_ids.reshape(-1)
    onehot = (flat_ids[:, None] == jnp.arange(experts, dtype=jnp.int32)[None, :]).astype(jnp.int32)
    before = jnp.cumsum(onehot, axis=0) - onehot
    slot_of = jnp.sum(before * onehot, axis=1)
    return flat_ids, slot_of


def contract_rows(left_op, right_op):
    return lax.dot_general(
        left_op, right_op, (((0,), (0,)), ((), ())), preferred_element_type=jnp.float32
    )


def contract_cols(left_op, right_op):
    return lax.dot_general(
        left_op, right_op, (((1,), (1,)), ((), ())), preferred_element_type=jnp.float32
    )


def shards(tokens, expert_ids, route_probs, w_gate, w_up, w_down, grad_out):
    senders = lax.axis_size("expert")
    tok_rows, model_width = tokens.shape
    top_count = expert_ids.shape[1]
    hidden_width = w_gate.shape[2]
    capacity = min(tok_rows, 4 * tok_rows * top_count // senders)
    total_rows = senders * capacity
    flat_ids, slot_of = route_slots(expert_ids, senders)
    token_of = jnp.arange(tok_rows * top_count, dtype=jnp.int32) // top_count

    packed = jnp.concatenate([w_gate[0], w_up[0], w_down[0].T], axis=1)
    whole = lax.all_gather(packed[None], "dp", axis=1, tiled=True)[0]
    gate_up = whole[:, : 2 * hidden_width]
    down_t = whole[:, 2 * hidden_width :]

    grad_wide = grad_out.astype(jnp.float32)
    scaled = (
        (route_probs[:, :, None] * grad_wide[:, None, :])
        .astype(jnp.bfloat16)
        .reshape(tok_rows * top_count, model_width)
    )
    base = flat_ids * (2 * capacity) + slot_of
    places = jnp.concatenate([base, base + capacity])
    values = jnp.concatenate([tokens[token_of], scaled], axis=0)
    outgoing = jnp.zeros((2 * total_rows, model_width), jnp.bfloat16).at[places].set(values)
    arrived = lax.all_to_all(
        outgoing.reshape(senders, 2 * capacity, model_width),
        "expert",
        split_axis=0,
        concat_axis=0,
        tiled=True,
    )
    slot_rows = arrived[:, :capacity].reshape(total_rows, model_width)
    grad_in = arrived[:, capacity:].reshape(total_rows, model_width)

    both_pre = jnp.dot(slot_rows, gate_up, preferred_element_type=jnp.float32)
    gate_pre = both_pre[:, :hidden_width]
    up_pre = both_pre[:, hidden_width:]
    sigmoid_g = jax.nn.sigmoid(gate_pre)
    activated = gate_pre * sigmoid_g
    hidden = (activated * up_pre).astype(jnp.bfloat16)
    back_hidden = jnp.dot(grad_in, down_t, preferred_element_type=jnp.float32)
    back_gate = (back_hidden * up_pre * sigmoid_g * (1.0 + gate_pre * (1.0 - sigmoid_g))).astype(
        jnp.bfloat16
    )
    back_up = (back_hidden * activated).astype(jnp.bfloat16)
    back_both = jnp.concatenate([back_gate, back_up], axis=1)

    grad_terms = jnp.concatenate(
        [
            contract_rows(slot_rows, back_both).astype(jnp.bfloat16),
            contract_rows(grad_in, hidden).astype(jnp.bfloat16),
        ],
        axis=1,
    )
    summed = lax.psum_scatter(grad_terms, "dp", scatter_dimension=0, tiled=True)

    expert_out = contract_cols(hidden, down_t).astype(jnp.bfloat16)
    back_rows = contract_cols(back_both, gate_up).astype(jnp.bfloat16)
    leaving = jnp.concatenate(
        [
            expert_out.reshape(senders, capacity, model_width),
            back_rows.reshape(senders, capacity, model_width),
        ],
        axis=1,
    )
    back_home = lax.all_to_all(leaving, "expert", split_axis=0, concat_axis=0, tiled=True)
    returned = back_home[:, :capacity]
    sent_back = back_home[:, capacity:]

    slot_place = flat_ids * capacity + slot_of
    picked = (
        returned.reshape(total_rows, model_width)[slot_place]
        .reshape(tok_rows, top_count, model_width)
        .astype(jnp.float32)
    )
    mixed_out = jnp.sum(route_probs[:, :, None] * picked, axis=1).astype(jnp.bfloat16)
    grad_probs = jnp.sum(grad_wide[:, None, :] * picked, axis=2)
    back_picked = sent_back.reshape(total_rows, model_width)[slot_place].reshape(
        tok_rows, top_count, model_width
    )
    grad_tokens = jnp.sum(back_picked.astype(jnp.float32), axis=1).astype(jnp.bfloat16)

    summed = summed.astype(jnp.float32).astype(jnp.bfloat16)
    grad_w_gate = summed[:, :hidden_width][None]
    grad_w_up = summed[:, hidden_width : 2 * hidden_width][None]
    grad_w_down = summed[:, 2 * hidden_width :].T[None]
    return (mixed_out, grad_tokens, grad_probs, grad_w_gate, grad_w_up, grad_w_down)


def solution(mesh):
    placed = (
        P(("dp", "expert"), None),
        P(("dp", "expert"), None),
        P(("dp", "expert"), None),
        P("expert", "dp", None),
        P("expert", "dp", None),
        P("expert", None, "dp"),
        P(("dp", "expert"), None),
    )
    return jax.shard_map(
        shards,
        mesh=mesh,
        in_specs=placed,
        out_specs=(
            P(("dp", "expert"), None),
            P(("dp", "expert"), None),
            P(("dp", "expert"), None),
            P("expert", "dp", None),
            P("expert", "dp", None),
            P("expert", None, "dp"),
        ),
        check_vma=False,
    )
```

```python
import jax
import jax.numpy as jnp
from jax import lax
from jax.sharding import PartitionSpec as P


def route_slots(expert_ids, experts):
    flat_ids = expert_ids.reshape(-1)
    onehot = (flat_ids[:, None] == jnp.arange(experts, dtype=jnp.int32)[None, :]).astype(jnp.int32)
    before = jnp.cumsum(onehot, axis=0) - onehot
    slot_of = jnp.sum(before * onehot, axis=1)
    return flat_ids, slot_of


def contract_rows(left_op, right_op):
    return lax.dot_general(
        left_op, right_op, (((0,), (0,)), ((), ())), preferred_element_type=jnp.float32
    )


def contract_cols(left_op, right_op):
    return lax.dot_general(
        left_op, right_op, (((1,), (1,)), ((), ())), preferred_element_type=jnp.float32
    )


def shards(tokens, expert_ids, route_probs, w_gate, w_up, w_down, grad_out):
    senders = lax.axis_size("expert")
    tok_rows, model_width = tokens.shape
    top_count = expert_ids.shape[1]
    hidden_width = w_gate.shape[2]
    capacity = min(tok_rows, 4 * tok_rows * top_count // senders)
    total_rows = senders * capacity
    flat_ids, slot_of = route_slots(expert_ids, senders)

    packed = jnp.concatenate([w_gate[0], w_up[0], w_down[0].T], axis=1)
    whole = lax.all_gather(packed[None], "dp", axis=1, tiled=True)[0]
    gate_up = whole[:, : 2 * hidden_width]
    down_t = whole[:, 2 * hidden_width :]

    grad_wide = grad_out.astype(jnp.float32)
    scaled = (
        (route_probs[:, :, None] * grad_wide[:, None, :])
        .astype(jnp.bfloat16)
        .reshape(tok_rows * top_count, model_width)
    )
    base = flat_ids * (2 * capacity) + slot_of
    slots = jnp.arange(2 * total_rows, dtype=jnp.int32)[:, None]
    pairs = base.reshape(tok_rows, top_count)
    pick_tok = (slots == pairs[None, :, 0]) | (slots == pairs[None, :, 1])
    pick_grad = slots == (base + capacity)[None, :]
    chooser = jnp.concatenate([pick_tok, pick_grad], axis=1).astype(jnp.bfloat16)
    sources = jnp.concatenate([tokens, scaled], axis=0)
    outgoing = jnp.dot(chooser, sources, preferred_element_type=jnp.float32).astype(jnp.bfloat16)
    arrived = lax.all_to_all(
        outgoing.reshape(senders, 2 * capacity, model_width),
        "expert",
        split_axis=0,
        concat_axis=0,
        tiled=True,
    )
    slot_rows = arrived[:, :capacity].reshape(total_rows, model_width)
    grad_in = arrived[:, capacity:].reshape(total_rows, model_width)

    both_pre = jnp.dot(slot_rows, gate_up, preferred_element_type=jnp.float32)
    gate_pre = both_pre[:, :hidden_width]
    up_pre = both_pre[:, hidden_width:]
    sigmoid_g = jax.nn.sigmoid(gate_pre)
    activated = gate_pre * sigmoid_g
    hidden = (activated * up_pre).astype(jnp.bfloat16)
    back_hidden = jnp.dot(grad_in, down_t, preferred_element_type=jnp.float32)
    back_gate = (back_hidden * up_pre * sigmoid_g * (1.0 + gate_pre * (1.0 - sigmoid_g))).astype(
        jnp.bfloat16
    )
    back_up = (back_hidden * activated).astype(jnp.bfloat16)
    back_both = jnp.concatenate([back_gate, back_up], axis=1)

    grad_terms = jnp.concatenate(
        [
            contract_rows(slot_rows, back_both).astype(jnp.bfloat16),
            contract_rows(grad_in, hidden).astype(jnp.bfloat16),
        ],
        axis=1,
    )
    summed = lax.psum_scatter(grad_terms, "dp", scatter_dimension=0, tiled=True)

    expert_out = contract_cols(hidden, down_t).astype(jnp.bfloat16)
    back_rows = contract_cols(back_both, gate_up).astype(jnp.bfloat16)
    leaving = jnp.concatenate(
        [
            expert_out.reshape(senders, capacity, model_width),
            back_rows.reshape(senders, capacity, model_width),
        ],
        axis=1,
    )
    back_home = lax.all_to_all(leaving, "expert", split_axis=0, concat_axis=0, tiled=True)

    home_flat = back_home.reshape(2 * total_rows, model_width)
    own_place = base.reshape(tok_rows, top_count).T.reshape(-1)
    picked = home_flat[own_place].reshape(top_count, tok_rows, model_width).astype(jnp.float32)
    back_picked = home_flat[own_place + capacity].reshape(top_count, tok_rows, model_width)
    probs_k = route_probs.T[:, :, None]
    mixed_out = jnp.sum(probs_k * picked, axis=0).astype(jnp.bfloat16)
    grad_probs = jnp.sum(grad_wide[None] * picked, axis=2).T
    grad_tokens = jnp.sum(back_picked.astype(jnp.float32), axis=0).astype(jnp.bfloat16)

    summed = summed.astype(jnp.float32).astype(jnp.bfloat16)
    grad_w_gate = summed[:, :hidden_width][None]
    grad_w_up = summed[:, hidden_width : 2 * hidden_width][None]
    grad_w_down = summed[:, 2 * hidden_width :].T[None]
    return (mixed_out, grad_tokens, grad_probs, grad_w_gate, grad_w_up, grad_w_down)


def solution(mesh):
    placed = (
        P(("dp", "expert"), None),
        P(("dp", "expert"), None),
        P(("dp", "expert"), None),
        P("expert", "dp", None),
        P("expert", "dp", None),
        P("expert", None, "dp"),
        P(("dp", "expert"), None),
    )
    return jax.shard_map(
        shards,
        mesh=mesh,
        in_specs=placed,
        out_specs=(
            P(("dp", "expert"), None),
            P(("dp", "expert"), None),
            P(("dp", "expert"), None),
            P("expert", "dp", None),
            P("expert", "dp", None),
            P("expert", None, "dp"),
        ),
        check_vma=False,
    )
```

```python
import jax
import jax.numpy as jnp
from jax import lax
from jax.sharding import PartitionSpec as P


def route_slots(expert_ids, experts):
    flat_ids = expert_ids.reshape(-1)
    onehot = (flat_ids[:, None] == jnp.arange(experts, dtype=jnp.int32)[None, :]).astype(jnp.int32)
    before = jnp.cumsum(onehot, axis=0) - onehot
    slot_of = jnp.sum(before * onehot, axis=1)
    return flat_ids, slot_of


def contract_rows(left_op, right_op):
    return lax.dot_general(
        left_op, right_op, (((0,), (0,)), ((), ())), preferred_element_type=jnp.float32
    )


def contract_cols(left_op, right_op):
    return lax.dot_general(
        left_op, right_op, (((1,), (1,)), ((), ())), preferred_element_type=jnp.float32
    )


def shards(tokens, expert_ids, route_probs, w_gate, w_up, w_down, grad_out):
    senders = lax.axis_size("expert")
    tok_rows, model_width = tokens.shape
    top_count = expert_ids.shape[1]
    hidden_width = w_gate.shape[2]
    capacity = min(tok_rows, 4 * tok_rows * top_count // senders)
    total_rows = senders * capacity
    flat_ids, slot_of = route_slots(expert_ids, senders)

    packed = jnp.concatenate([w_gate[0], w_up[0], w_down[0].T], axis=1)
    whole = lax.all_gather(packed[None], "dp", axis=1, tiled=True)[0]
    gate_up = whole[:, : 2 * hidden_width]
    down_t = whole[:, 2 * hidden_width :]

    grad_wide = grad_out.astype(jnp.float32)
    scaled = (
        (route_probs[:, :, None] * grad_wide[:, None, :])
        .astype(jnp.bfloat16)
        .reshape(tok_rows * top_count, model_width)
    )
    base = flat_ids * (2 * capacity) + slot_of
    slots = jnp.arange(2 * total_rows, dtype=jnp.int32)[:, None]
    pairs = base.reshape(tok_rows, top_count)
    pick_tok = (slots == pairs[None, :, 0]) | (slots == pairs[None, :, 1])
    pick_grad = slots == (base + capacity)[None, :]
    chooser = jnp.concatenate([pick_tok, pick_grad], axis=1).astype(jnp.bfloat16)
    sources = jnp.concatenate([tokens, scaled], axis=0)
    outgoing = jnp.dot(chooser, sources, preferred_element_type=jnp.float32).astype(jnp.bfloat16)
    arrived = lax.all_to_all(
        outgoing.reshape(senders, 2 * capacity, model_width),
        "expert",
        split_axis=0,
        concat_axis=0,
        tiled=True,
    )
    slot_rows = arrived[:, :capacity].reshape(total_rows, model_width)
    grad_in = arrived[:, capacity:].reshape(total_rows, model_width)

    both_pre = jnp.dot(slot_rows, gate_up, preferred_element_type=jnp.float32)
    gate_pre = both_pre[:, :hidden_width]
    up_pre = both_pre[:, hidden_width:]
    sigmoid_g = jax.nn.sigmoid(gate_pre)
    activated = gate_pre * sigmoid_g
    hidden = (activated * up_pre).astype(jnp.bfloat16)
    back_hidden = jnp.dot(grad_in, down_t, preferred_element_type=jnp.float32)
    back_gate = (back_hidden * up_pre * sigmoid_g * (1.0 + gate_pre * (1.0 - sigmoid_g))).astype(
        jnp.bfloat16
    )
    back_up = (back_hidden * activated).astype(jnp.bfloat16)
    back_both = jnp.concatenate([back_gate, back_up], axis=1)

    grad_terms = jnp.concatenate(
        [
            contract_rows(slot_rows, back_both).astype(jnp.bfloat16),
            contract_rows(grad_in, hidden).astype(jnp.bfloat16),
        ],
        axis=1,
    )
    summed = lax.psum_scatter(grad_terms, "dp", scatter_dimension=0, tiled=True)

    expert_out = contract_cols(hidden, down_t).astype(jnp.bfloat16)
    back_rows = contract_cols(back_both, gate_up).astype(jnp.bfloat16)
    leaving = jnp.concatenate(
        [
            expert_out.reshape(senders, capacity, model_width),
            back_rows.reshape(senders, capacity, model_width),
        ],
        axis=1,
    )
    back_home = lax.all_to_all(leaving, "expert", split_axis=0, concat_axis=0, tiled=True)

    home_flat = back_home.reshape(2 * total_rows, model_width)
    own_place = base.reshape(tok_rows, top_count).T.reshape(-1)
    wanted = jnp.concatenate([own_place, own_place + capacity])
    taker = (jnp.arange(2 * total_rows, dtype=jnp.int32)[None, :] == wanted[:, None]).astype(
        jnp.bfloat16
    )
    taken = jnp.dot(taker, home_flat, preferred_element_type=jnp.float32)
    picked = taken[: tok_rows * top_count].reshape(top_count, tok_rows, model_width)
    back_picked = taken[tok_rows * top_count :].reshape(top_count, tok_rows, model_width)
    probs_k = route_probs.T[:, :, None]
    mixed_out = jnp.sum(probs_k * picked, axis=0).astype(jnp.bfloat16)
    grad_probs = jnp.sum(grad_wide[None] * picked, axis=2).T
    grad_tokens = jnp.sum(back_picked.astype(jnp.float32), axis=0).astype(jnp.bfloat16)

    grad_w_gate = summed[:, :hidden_width][None]
    grad_w_up = summed[:, hidden_width : 2 * hidden_width][None]
    grad_w_down = summed[:, 2 * hidden_width :].T[None]
    return (mixed_out, grad_tokens, grad_probs, grad_w_gate, grad_w_up, grad_w_down)


def solution(mesh):
    placed = (
        P(("dp", "expert"), None),
        P(("dp", "expert"), None),
        P(("dp", "expert"), None),
        P("expert", "dp", None),
        P("expert", "dp", None),
        P("expert", None, "dp"),
        P(("dp", "expert"), None),
    )
    return jax.shard_map(
        shards,
        mesh=mesh,
        in_specs=placed,
        out_specs=(
            P(("dp", "expert"), None),
            P(("dp", "expert"), None),
            P(("dp", "expert"), None),
            P("expert", "dp", None),
            P("expert", "dp", None),
            P("expert", None, "dp"),
        ),
        check_vma=False,
    )
```

```python
import jax
import jax.numpy as jnp
from jax import lax
from jax.sharding import PartitionSpec as P


def route_slots(expert_ids, experts):
    flat_ids = expert_ids.reshape(-1)
    onehot = (flat_ids[:, None] == jnp.arange(experts, dtype=jnp.int32)[None, :]).astype(jnp.int32)
    before = jnp.cumsum(onehot, axis=0) - onehot
    slot_of = jnp.sum(before * onehot, axis=1)
    return flat_ids, slot_of


def contract_rows(left_op, right_op):
    return lax.dot_general(
        left_op, right_op, (((0,), (0,)), ((), ())), preferred_element_type=jnp.float32
    )


def contract_cols(left_op, right_op):
    return lax.dot_general(
        left_op, right_op, (((1,), (1,)), ((), ())), preferred_element_type=jnp.float32
    )


def shards(tokens, expert_ids, route_probs, w_gate, w_up, w_down, grad_out):
    senders = lax.axis_size("expert")
    tok_rows, model_width = tokens.shape
    top_count = expert_ids.shape[1]
    hidden_width = w_gate.shape[2]
    capacity = min(tok_rows, 4 * tok_rows * top_count // senders)
    total_rows = senders * capacity
    flat_ids, slot_of = route_slots(expert_ids, senders)

    packed = jnp.concatenate([w_gate[0], w_up[0], w_down[0].T], axis=1)
    whole = lax.all_gather(packed[None], "dp", axis=1, tiled=True)[0]
    gate_up = whole[:, : 2 * hidden_width]
    down_t = whole[:, 2 * hidden_width :]

    grad_wide = grad_out.astype(jnp.float32)
    scaled = (
        (route_probs[:, :, None] * grad_wide[:, None, :])
        .astype(jnp.bfloat16)
        .reshape(tok_rows * top_count, model_width)
    )
    base = flat_ids * (2 * capacity) + slot_of
    slots = jnp.arange(2 * total_rows, dtype=jnp.int32)[:, None]
    pairs = base.reshape(tok_rows, top_count)
    pick_tok = (slots == pairs[None, :, 0]) | (slots == pairs[None, :, 1])
    pick_grad = slots == (base + capacity)[None, :]
    chooser = jnp.concatenate([pick_tok, pick_grad], axis=1).astype(jnp.bfloat16)
    sources = jnp.concatenate([tokens, scaled], axis=0)
    outgoing = jnp.dot(chooser, sources, preferred_element_type=jnp.float32).astype(jnp.bfloat16)
    arrived = lax.all_to_all(
        outgoing.reshape(senders, 2 * capacity, model_width),
        "expert",
        split_axis=0,
        concat_axis=0,
        tiled=True,
    )
    slot_rows = arrived[:, :capacity].reshape(total_rows, model_width)
    grad_in = arrived[:, capacity:].reshape(total_rows, model_width)

    both_pre = jnp.dot(slot_rows, gate_up, preferred_element_type=jnp.float32)
    gate_pre = both_pre[:, :hidden_width]
    up_pre = both_pre[:, hidden_width:]
    sigmoid_g = jax.nn.sigmoid(gate_pre)
    activated = gate_pre * sigmoid_g
    hidden = (activated * up_pre).astype(jnp.bfloat16)
    back_hidden = jnp.dot(grad_in, down_t, preferred_element_type=jnp.float32)
    back_gate = (back_hidden * up_pre * sigmoid_g * (1.0 + gate_pre * (1.0 - sigmoid_g))).astype(
        jnp.bfloat16
    )
    back_up = (back_hidden * activated).astype(jnp.bfloat16)
    back_both = jnp.concatenate([back_gate, back_up], axis=1)

    grad_terms = jnp.concatenate(
        [
            contract_rows(slot_rows, back_both).astype(jnp.bfloat16),
            contract_rows(grad_in, hidden).astype(jnp.bfloat16),
        ],
        axis=1,
    )
    summed = lax.psum_scatter(grad_terms, "dp", scatter_dimension=0, tiled=True)

    expert_out = contract_cols(hidden, down_t).astype(jnp.bfloat16)
    back_rows = contract_cols(back_both, gate_up).astype(jnp.bfloat16)
    leaving = jnp.concatenate(
        [
            expert_out.reshape(senders, capacity, model_width),
            back_rows.reshape(senders, capacity, model_width),
        ],
        axis=1,
    )
    back_home = lax.all_to_all(leaving, "expert", split_axis=0, concat_axis=0, tiled=True)

    back_home, summed = lax.optimization_barrier((back_home, summed))
    home_flat = back_home.reshape(2 * total_rows, model_width)
    own_place = base.reshape(tok_rows, top_count).T.reshape(-1)
    wanted = jnp.concatenate([own_place, own_place + capacity])
    taker = (jnp.arange(2 * total_rows, dtype=jnp.int32)[None, :] == wanted[:, None]).astype(
        jnp.bfloat16
    )
    taken = jnp.dot(taker, home_flat, preferred_element_type=jnp.float32)
    picked = taken[: tok_rows * top_count].reshape(top_count, tok_rows, model_width)
    back_picked = taken[tok_rows * top_count :].reshape(top_count, tok_rows, model_width)
    probs_k = route_probs.T[:, :, None]
    mixed_out = jnp.sum(probs_k * picked, axis=0).astype(jnp.bfloat16)
    grad_probs = jnp.sum(grad_wide[None] * picked, axis=2).T
    grad_tokens = jnp.sum(back_picked.astype(jnp.float32), axis=0).astype(jnp.bfloat16)

    grad_w_gate = summed[:, :hidden_width][None]
    grad_w_up = summed[:, hidden_width : 2 * hidden_width][None]
    grad_w_down = summed[:, 2 * hidden_width :].T[None]
    return (mixed_out, grad_tokens, grad_probs, grad_w_gate, grad_w_up, grad_w_down)


def solution(mesh):
    placed = (
        P(("dp", "expert"), None),
        P(("dp", "expert"), None),
        P(("dp", "expert"), None),
        P("expert", "dp", None),
        P("expert", "dp", None),
        P("expert", None, "dp"),
        P(("dp", "expert"), None),
    )
    return jax.shard_map(
        shards,
        mesh=mesh,
        in_specs=placed,
        out_specs=(
            P(("dp", "expert"), None),
            P(("dp", "expert"), None),
            P(("dp", "expert"), None),
            P("expert", "dp", None),
            P("expert", "dp", None),
            P("expert", None, "dp"),
        ),
        check_vma=False,
    )
```

```python
import jax
import jax.numpy as jnp
from jax import lax
from jax.sharding import PartitionSpec as P


def route_slots(expert_ids, experts):
    flat_ids = expert_ids.reshape(-1)
    onehot = (flat_ids[:, None] == jnp.arange(experts, dtype=jnp.int32)[None, :]).astype(jnp.int32)
    before = jnp.cumsum(onehot, axis=0) - onehot
    slot_of = jnp.sum(before * onehot, axis=1)
    return flat_ids, slot_of


def contract_rows(left_op, right_op):
    return lax.dot_general(
        left_op, right_op, (((0,), (0,)), ((), ())), preferred_element_type=jnp.float32
    )


def contract_cols(left_op, right_op):
    return lax.dot_general(
        left_op, right_op, (((1,), (1,)), ((), ())), preferred_element_type=jnp.float32
    )


def shards(tokens, expert_ids, route_probs, w_gate, w_up, w_down, grad_out):
    senders = lax.axis_size("expert")
    tok_rows, model_width = tokens.shape
    top_count = expert_ids.shape[1]
    hidden_width = w_gate.shape[2]
    capacity = min(tok_rows, 4 * tok_rows * top_count // senders)
    total_rows = senders * capacity
    flat_ids, slot_of = route_slots(expert_ids, senders)

    packed = jnp.concatenate([w_gate[0], w_up[0], w_down[0].T], axis=1)
    whole = lax.all_gather(packed[None], "dp", axis=1, tiled=True)[0]
    gate_up = whole[:, : 2 * hidden_width]
    down_t = whole[:, 2 * hidden_width :]

    grad_wide = grad_out.astype(jnp.float32)
    scaled = (
        (route_probs.T[:, :, None] * grad_wide[None])
        .astype(jnp.bfloat16)
        .reshape(tok_rows * top_count, model_width)
    )
    base = flat_ids * (2 * capacity) + slot_of
    slots = jnp.arange(2 * total_rows, dtype=jnp.int32)[:, None]
    pairs = base.reshape(tok_rows, top_count)
    pick_tok = (slots == pairs[None, :, 0]) | (slots == pairs[None, :, 1])
    pick_grad = slots == (pairs.T.reshape(-1) + capacity)[None, :]
    chooser = jnp.concatenate([pick_tok, pick_grad], axis=1).astype(jnp.bfloat16)
    sources = jnp.concatenate([tokens, scaled], axis=0)
    outgoing = jnp.dot(chooser, sources, preferred_element_type=jnp.float32).astype(jnp.bfloat16)
    arrived = lax.all_to_all(
        outgoing.reshape(senders, 2 * capacity, model_width),
        "expert",
        split_axis=0,
        concat_axis=0,
        tiled=True,
    )
    arrived, whole = lax.optimization_barrier((arrived, whole))
    slot_rows = arrived[:, :capacity].reshape(total_rows, model_width)
    grad_in = arrived[:, capacity:].reshape(total_rows, model_width)

    both_pre = jnp.dot(slot_rows, gate_up, preferred_element_type=jnp.float32)
    gate_pre = both_pre[:, :hidden_width]
    up_pre = both_pre[:, hidden_width:]
    sigmoid_g = jax.nn.sigmoid(gate_pre)
    activated = gate_pre * sigmoid_g
    hidden = (activated * up_pre).astype(jnp.bfloat16)
    back_hidden = jnp.dot(grad_in, down_t, preferred_element_type=jnp.float32)
    back_gate = (back_hidden * up_pre * sigmoid_g * (1.0 + gate_pre * (1.0 - sigmoid_g))).astype(
        jnp.bfloat16
    )
    back_up = (back_hidden * activated).astype(jnp.bfloat16)
    back_both = jnp.concatenate([back_gate, back_up], axis=1)

    grad_terms = jnp.concatenate(
        [
            contract_rows(slot_rows, back_both).astype(jnp.bfloat16),
            contract_rows(grad_in, hidden).astype(jnp.bfloat16),
        ],
        axis=1,
    )
    summed = lax.psum_scatter(grad_terms, "dp", scatter_dimension=0, tiled=True)

    expert_out = contract_cols(hidden, down_t).astype(jnp.bfloat16)
    back_rows = contract_cols(back_both, gate_up).astype(jnp.bfloat16)
    leaving = jnp.concatenate(
        [
            expert_out.reshape(senders, capacity, model_width),
            back_rows.reshape(senders, capacity, model_width),
        ],
        axis=1,
    )
    back_home = lax.all_to_all(leaving, "expert", split_axis=0, concat_axis=0, tiled=True)

    back_home, summed = lax.optimization_barrier((back_home, summed))
    home_flat = back_home.reshape(2 * total_rows, model_width)
    own_place = base.reshape(tok_rows, top_count).T.reshape(-1)
    wanted = jnp.concatenate([own_place, own_place + capacity])
    taker = (jnp.arange(2 * total_rows, dtype=jnp.int32)[None, :] == wanted[:, None]).astype(
        jnp.bfloat16
    )
    taken = jnp.dot(taker, home_flat, preferred_element_type=jnp.float32)
    picked = taken[: tok_rows * top_count].reshape(top_count, tok_rows, model_width)
    back_picked = taken[tok_rows * top_count :].reshape(top_count, tok_rows, model_width)
    probs_k = route_probs.T[:, :, None]
    mixed_out = jnp.sum(probs_k * picked, axis=0).astype(jnp.bfloat16)
    grad_probs = jnp.sum(grad_wide[None] * picked, axis=2).T
    grad_tokens = jnp.sum(back_picked.astype(jnp.float32), axis=0).astype(jnp.bfloat16)

    grad_w_gate = summed[:, :hidden_width][None]
    grad_w_up = summed[:, hidden_width : 2 * hidden_width][None]
    grad_w_down = summed[:, 2 * hidden_width :].T[None]
    return (mixed_out, grad_tokens, grad_probs, grad_w_gate, grad_w_up, grad_w_down)


def solution(mesh):
    placed = (
        P(("dp", "expert"), None),
        P(("dp", "expert"), None),
        P(("dp", "expert"), None),
        P("expert", "dp", None),
        P("expert", "dp", None),
        P("expert", None, "dp"),
        P(("dp", "expert"), None),
    )
    return jax.shard_map(
        shards,
        mesh=mesh,
        in_specs=placed,
        out_specs=(
            P(("dp", "expert"), None),
            P(("dp", "expert"), None),
            P(("dp", "expert"), None),
            P("expert", "dp", None),
            P("expert", "dp", None),
            P("expert", None, "dp"),
        ),
        check_vma=False,
    )
```

```python
import jax
import jax.numpy as jnp
from jax import lax
from jax.sharding import PartitionSpec as P


def route_slots(expert_ids, experts):
    flat_ids = expert_ids.reshape(-1)
    onehot = (flat_ids[:, None] == jnp.arange(experts, dtype=jnp.int32)[None, :]).astype(jnp.int32)
    before = jnp.cumsum(onehot, axis=0) - onehot
    slot_of = jnp.sum(before * onehot, axis=1)
    return flat_ids, slot_of


def contract_rows(left_op, right_op):
    return lax.dot_general(
        left_op, right_op, (((0,), (0,)), ((), ())), preferred_element_type=jnp.float32
    )


def contract_cols(left_op, right_op):
    return lax.dot_general(
        left_op, right_op, (((1,), (1,)), ((), ())), preferred_element_type=jnp.float32
    )


def shards(tokens, expert_ids, route_probs, w_gate, w_up, w_down, grad_out):
    senders = lax.axis_size("expert")
    tok_rows, model_width = tokens.shape
    top_count = expert_ids.shape[1]
    hidden_width = w_gate.shape[2]
    capacity = min(tok_rows, 4 * tok_rows * top_count // senders)
    total_rows = senders * capacity
    flat_ids, slot_of = route_slots(expert_ids, senders)

    packed = jnp.concatenate([w_gate[0], w_up[0], w_down[0].T], axis=1)
    whole = lax.all_gather(packed[None], "dp", axis=1, tiled=True)[0]
    grad_wide = grad_out.astype(jnp.float32)
    scaled = (
        (route_probs.T[:, :, None] * grad_wide[None])
        .astype(jnp.bfloat16)
        .reshape(tok_rows * top_count, model_width)
    )
    base = flat_ids * (2 * capacity) + slot_of
    place = flat_ids * capacity + slot_of
    slots = jnp.arange(total_rows, dtype=jnp.int32)[:, None]
    pairs = place.reshape(tok_rows, top_count)
    pick_tok = ((slots == pairs[None, :, 0]) | (slots == pairs[None, :, 1])).astype(jnp.bfloat16)
    pick_grad = (slots == pairs.T.reshape(-1)[None, :]).astype(jnp.bfloat16)
    tok_send = jnp.dot(pick_tok, tokens, preferred_element_type=jnp.float32).astype(jnp.bfloat16)
    grad_send = jnp.dot(pick_grad, scaled, preferred_element_type=jnp.float32).astype(jnp.bfloat16)
    slot_rows, grad_in = (
        lax.all_to_all(
            sent.reshape(senders, capacity, model_width),
            "expert",
            split_axis=0,
            concat_axis=0,
            tiled=True,
        ).reshape(total_rows, model_width)
        for sent in (tok_send, grad_send)
    )
    slot_rows, grad_in, whole = lax.optimization_barrier((slot_rows, grad_in, whole))
    gate_up = whole[:, : 2 * hidden_width]
    down_t = whole[:, 2 * hidden_width :]

    both_pre = jnp.dot(slot_rows, gate_up, preferred_element_type=jnp.float32)
    gate_pre = both_pre[:, :hidden_width]
    up_pre = both_pre[:, hidden_width:]
    sigmoid_g = jax.nn.sigmoid(gate_pre)
    activated = gate_pre * sigmoid_g
    hidden = (activated * up_pre).astype(jnp.bfloat16)
    back_hidden = jnp.dot(grad_in, down_t, preferred_element_type=jnp.float32)
    back_gate = (back_hidden * up_pre * sigmoid_g * (1.0 + gate_pre * (1.0 - sigmoid_g))).astype(
        jnp.bfloat16
    )
    back_up = (back_hidden * activated).astype(jnp.bfloat16)
    back_both = jnp.concatenate([back_gate, back_up], axis=1)

    grad_terms = jnp.concatenate(
        [
            contract_rows(slot_rows, back_both).astype(jnp.bfloat16),
            contract_rows(grad_in, hidden).astype(jnp.bfloat16),
        ],
        axis=1,
    )
    summed = lax.psum_scatter(grad_terms, "dp", scatter_dimension=0, tiled=True)

    expert_out = contract_cols(hidden, down_t).astype(jnp.bfloat16)
    back_rows = contract_cols(back_both, gate_up).astype(jnp.bfloat16)
    leaving = jnp.concatenate(
        [
            expert_out.reshape(senders, capacity, model_width),
            back_rows.reshape(senders, capacity, model_width),
        ],
        axis=1,
    )
    back_home = lax.all_to_all(leaving, "expert", split_axis=0, concat_axis=0, tiled=True)

    back_home, summed = lax.optimization_barrier((back_home, summed))
    home_flat = back_home.reshape(2 * total_rows, model_width)
    own_place = base.reshape(tok_rows, top_count).T.reshape(-1)
    wanted = jnp.concatenate([own_place, own_place + capacity])
    taker = (jnp.arange(2 * total_rows, dtype=jnp.int32)[None, :] == wanted[:, None]).astype(
        jnp.bfloat16
    )
    taken = jnp.dot(taker, home_flat, preferred_element_type=jnp.float32)
    picked = taken[: tok_rows * top_count].reshape(top_count, tok_rows, model_width)
    back_picked = taken[tok_rows * top_count :].reshape(top_count, tok_rows, model_width)
    probs_k = route_probs.T[:, :, None]
    mixed_out = jnp.sum(probs_k * picked, axis=0).astype(jnp.bfloat16)
    grad_probs = jnp.sum(grad_wide[None] * picked, axis=2).T
    grad_tokens = jnp.sum(back_picked.astype(jnp.float32), axis=0).astype(jnp.bfloat16)

    grad_w_gate = summed[:, :hidden_width][None]
    grad_w_up = summed[:, hidden_width : 2 * hidden_width][None]
    grad_w_down = summed[:, 2 * hidden_width :].T[None]
    return (mixed_out, grad_tokens, grad_probs, grad_w_gate, grad_w_up, grad_w_down)


def solution(mesh):
    placed = (
        P(("dp", "expert"), None),
        P(("dp", "expert"), None),
        P(("dp", "expert"), None),
        P("expert", "dp", None),
        P("expert", "dp", None),
        P("expert", None, "dp"),
        P(("dp", "expert"), None),
    )
    return jax.shard_map(
        shards,
        mesh=mesh,
        in_specs=placed,
        out_specs=(
            P(("dp", "expert"), None),
            P(("dp", "expert"), None),
            P(("dp", "expert"), None),
            P("expert", "dp", None),
            P("expert", "dp", None),
            P("expert", None, "dp"),
        ),
        check_vma=False,
    )
```

```python
import jax
import jax.numpy as jnp
from jax import lax
from jax.sharding import PartitionSpec as P


def route_slots(expert_ids, experts):
    flat_ids = expert_ids.reshape(-1)
    onehot = (flat_ids[:, None] == jnp.arange(experts, dtype=jnp.int32)[None, :]).astype(jnp.int32)
    before = jnp.cumsum(onehot, axis=0) - onehot
    slot_of = jnp.sum(before * onehot, axis=1)
    return flat_ids, slot_of


def contract_rows(left_op, right_op):
    return lax.dot_general(
        left_op, right_op, (((0,), (0,)), ((), ())), preferred_element_type=jnp.float32
    )


def contract_cols(left_op, right_op):
    return lax.dot_general(
        left_op, right_op, (((1,), (1,)), ((), ())), preferred_element_type=jnp.float32
    )


def shards(tokens, expert_ids, route_probs, w_gate, w_up, w_down, grad_out):
    senders = lax.axis_size("expert")
    tok_rows, model_width = tokens.shape
    top_count = expert_ids.shape[1]
    hidden_width = w_gate.shape[2]
    capacity = min(tok_rows, 4 * tok_rows * top_count // senders)
    total_rows = senders * capacity
    flat_ids, slot_of = route_slots(expert_ids, senders)

    packed = jnp.concatenate([w_gate[0], w_up[0], w_down[0].T], axis=1)
    whole = lax.all_gather(packed[None], "dp", axis=1, tiled=True)[0]
    gate_up = whole[:, : 2 * hidden_width]
    down_t = whole[:, 2 * hidden_width :]

    grad_wide = grad_out.astype(jnp.float32)
    scaled = (
        (route_probs.T[:, :, None] * grad_wide[None])
        .astype(jnp.bfloat16)
        .reshape(tok_rows * top_count, model_width)
    )
    base = flat_ids * (2 * capacity) + slot_of
    slots = jnp.arange(2 * total_rows, dtype=jnp.int32)[:, None]
    pairs = base.reshape(tok_rows, top_count)
    pick_tok = (slots == pairs[None, :, 0]) | (slots == pairs[None, :, 1])
    pick_grad = slots == (pairs.T.reshape(-1) + capacity)[None, :]
    chooser = jnp.concatenate([pick_tok, pick_grad], axis=1).astype(jnp.bfloat16)
    sources = jnp.concatenate([tokens, scaled], axis=0)
    outgoing = jnp.dot(chooser, sources, preferred_element_type=jnp.float32).astype(jnp.bfloat16)
    arrived = lax.all_to_all(
        outgoing.reshape(senders, 2 * capacity, model_width),
        "expert",
        split_axis=0,
        concat_axis=0,
        tiled=True,
    )
    arrived, whole = lax.optimization_barrier((arrived, whole))
    slot_rows = arrived[:, :capacity].reshape(total_rows, model_width)
    grad_in = arrived[:, capacity:].reshape(total_rows, model_width)

    both_pre = jnp.dot(slot_rows, gate_up, preferred_element_type=jnp.float32)
    gate_pre = both_pre[:, :hidden_width]
    up_pre = both_pre[:, hidden_width:]
    sigmoid_g = jax.nn.sigmoid(gate_pre)
    activated = gate_pre * sigmoid_g
    hidden = (activated * up_pre).astype(jnp.bfloat16)
    back_hidden = jnp.dot(grad_in, down_t, preferred_element_type=jnp.float32)
    back_gate = (back_hidden * up_pre * sigmoid_g * (1.0 + gate_pre * (1.0 - sigmoid_g))).astype(
        jnp.bfloat16
    )
    back_up = (back_hidden * activated).astype(jnp.bfloat16)
    back_both = jnp.concatenate([back_gate, back_up], axis=1)

    grad_terms = jnp.concatenate(
        [
            contract_rows(slot_rows, back_both).astype(jnp.bfloat16),
            contract_rows(grad_in, hidden).astype(jnp.bfloat16),
        ],
        axis=1,
    )
    summed = lax.psum_scatter(grad_terms, "dp", scatter_dimension=0, tiled=True)

    expert_out = contract_cols(hidden, down_t).astype(jnp.bfloat16)
    back_rows = contract_cols(back_both, gate_up).astype(jnp.bfloat16)
    leaving = jnp.concatenate(
        [
            expert_out.reshape(senders, capacity, model_width),
            back_rows.reshape(senders, capacity, model_width),
        ],
        axis=1,
    )
    back_home = lax.all_to_all(leaving, "expert", split_axis=0, concat_axis=0, tiled=True)

    back_home, summed = lax.optimization_barrier((back_home, summed))
    own_place = (flat_ids * capacity + slot_of).reshape(tok_rows, top_count).T.reshape(-1)
    taker = (jnp.arange(total_rows, dtype=jnp.int32)[None, :] == own_place[:, None]).astype(
        jnp.bfloat16
    ).reshape(tok_rows * top_count, senders, capacity)
    picked, back_picked = (
        lax.dot_general(
            taker,
            back_home[:, half * capacity : (half + 1) * capacity],
            (((1, 2), (0, 1)), ((), ())),
            preferred_element_type=jnp.float32,
        ).reshape(top_count, tok_rows, model_width)
        for half in (0, 1)
    )
    probs_k = route_probs.T[:, :, None]
    mixed_out = jnp.sum(probs_k * picked, axis=0).astype(jnp.bfloat16)
    grad_probs = jnp.sum(grad_wide[None] * picked, axis=2).T
    grad_tokens = jnp.sum(back_picked.astype(jnp.float32), axis=0).astype(jnp.bfloat16)

    grad_w_gate = summed[:, :hidden_width][None]
    grad_w_up = summed[:, hidden_width : 2 * hidden_width][None]
    grad_w_down = summed[:, 2 * hidden_width :].T[None]
    return (mixed_out, grad_tokens, grad_probs, grad_w_gate, grad_w_up, grad_w_down)


def solution(mesh):
    placed = (
        P(("dp", "expert"), None),
        P(("dp", "expert"), None),
        P(("dp", "expert"), None),
        P("expert", "dp", None),
        P("expert", "dp", None),
        P("expert", None, "dp"),
        P(("dp", "expert"), None),
    )
    return jax.shard_map(
        shards,
        mesh=mesh,
        in_specs=placed,
        out_specs=(
            P(("dp", "expert"), None),
            P(("dp", "expert"), None),
            P(("dp", "expert"), None),
            P("expert", "dp", None),
            P("expert", "dp", None),
            P("expert", None, "dp"),
        ),
        check_vma=False,
    )
```

```python
import jax
import jax.numpy as jnp
from jax import lax
from jax.sharding import PartitionSpec as P


def route_slots(expert_ids, experts):
    flat_ids = expert_ids.reshape(-1)
    onehot = (flat_ids[:, None] == jnp.arange(experts, dtype=jnp.int32)[None, :]).astype(jnp.int32)
    before = jnp.cumsum(onehot, axis=0) - onehot
    slot_of = jnp.sum(before * onehot, axis=1)
    return flat_ids, slot_of


def contract_rows(left_op, right_op):
    return lax.dot_general(
        left_op, right_op, (((0,), (0,)), ((), ())), preferred_element_type=jnp.float32
    )


def contract_cols(left_op, right_op):
    return lax.dot_general(
        left_op, right_op, (((1,), (1,)), ((), ())), preferred_element_type=jnp.float32
    )


def shards(tokens, expert_ids, route_probs, w_gate, w_up, w_down, grad_out):
    senders = lax.axis_size("expert")
    tok_rows, model_width = tokens.shape
    top_count = expert_ids.shape[1]
    hidden_width = w_gate.shape[2]
    capacity = min(tok_rows, 4 * tok_rows * top_count // senders)
    total_rows = senders * capacity
    flat_ids, slot_of = route_slots(expert_ids, senders)

    packed = jnp.concatenate([w_gate[0], w_up[0], w_down[0].T], axis=1)
    whole = lax.all_gather(packed[None], "dp", axis=1, tiled=True)[0]
    gate_up = whole[:, : 2 * hidden_width]
    down_t = whole[:, 2 * hidden_width :]

    grad_wide = grad_out.astype(jnp.float32)
    scaled = (
        (route_probs.T[:, :, None] * grad_wide[None])
        .astype(jnp.bfloat16)
        .reshape(tok_rows * top_count, model_width)
    )
    base = flat_ids * (2 * capacity) + slot_of
    slots = jnp.arange(2 * total_rows, dtype=jnp.int32)[:, None]
    pairs = base.reshape(tok_rows, top_count)
    pick_tok = (slots == pairs[None, :, 0]) | (slots == pairs[None, :, 1])
    pick_grad = slots == (pairs.T.reshape(-1) + capacity)[None, :]
    chooser = jnp.concatenate([pick_tok, pick_grad], axis=1).astype(jnp.bfloat16)
    sources = jnp.concatenate([tokens, scaled], axis=0)
    outgoing = jnp.dot(chooser, sources, preferred_element_type=jnp.float32).astype(jnp.bfloat16)
    arrived = lax.all_to_all(
        outgoing.reshape(senders, 2 * capacity, model_width),
        "expert",
        split_axis=0,
        concat_axis=0,
        tiled=True,
    )
    arrived, whole = lax.optimization_barrier((arrived, whole))
    slot_rows = arrived[:, :capacity].reshape(total_rows, model_width)
    grad_in = arrived[:, capacity:].reshape(total_rows, model_width)

    both_pre = jnp.dot(slot_rows, gate_up, preferred_element_type=jnp.float32)
    gate_pre = both_pre[:, :hidden_width]
    up_pre = both_pre[:, hidden_width:]
    sigmoid_g = jax.nn.sigmoid(gate_pre)
    activated = gate_pre * sigmoid_g
    hidden = (activated * up_pre).astype(jnp.bfloat16)
    back_hidden = jnp.dot(grad_in, down_t, preferred_element_type=jnp.float32)
    back_gate = (back_hidden * up_pre * sigmoid_g * (1.0 + gate_pre * (1.0 - sigmoid_g))).astype(
        jnp.bfloat16
    )
    back_up = (back_hidden * activated).astype(jnp.bfloat16)
    back_both = jnp.concatenate([back_gate, back_up], axis=1)

    grad_terms = jnp.concatenate(
        [
            contract_rows(slot_rows, back_both).astype(jnp.bfloat16),
            contract_rows(grad_in, hidden).astype(jnp.bfloat16),
        ],
        axis=1,
    )
    summed = lax.psum_scatter(grad_terms, "dp", scatter_dimension=0, tiled=True)

    expert_out = contract_cols(hidden, down_t).astype(jnp.bfloat16)
    back_rows = contract_cols(back_both, gate_up).astype(jnp.bfloat16)
    leaving = jnp.concatenate(
        [
            expert_out.reshape(senders, capacity, model_width),
            back_rows.reshape(senders, capacity, model_width),
        ],
        axis=1,
    )
    back_home = lax.all_to_all(leaving, "expert", split_axis=0, concat_axis=0, tiled=True)

    back_home, gate_sum, up_sum, down_sum = lax.optimization_barrier(
        (
            back_home,
            summed[:, :hidden_width],
            summed[:, hidden_width : 2 * hidden_width],
            summed[:, 2 * hidden_width :],
        )
    )
    own_place = (flat_ids * capacity + slot_of).reshape(tok_rows, top_count).T.reshape(-1)
    taker = (jnp.arange(total_rows, dtype=jnp.int32)[None, :] == own_place[:, None]).astype(
        jnp.bfloat16
    ).reshape(tok_rows * top_count, senders, capacity)
    picked, back_picked = (
        lax.dot_general(
            taker,
            back_home[:, half * capacity : (half + 1) * capacity],
            (((1, 2), (0, 1)), ((), ())),
            preferred_element_type=jnp.float32,
        ).reshape(top_count, tok_rows, model_width)
        for half in (0, 1)
    )
    probs_k = route_probs.T[:, :, None]
    mixed_out = jnp.sum(probs_k * picked, axis=0).astype(jnp.bfloat16)
    grad_probs = jnp.sum(grad_wide[None] * picked, axis=2).T
    grad_tokens = jnp.sum(back_picked.astype(jnp.float32), axis=0).astype(jnp.bfloat16)

    grad_w_gate = gate_sum[None]
    grad_w_up = up_sum[None]
    grad_w_down = down_sum.T[None]
    return (mixed_out, grad_tokens, grad_probs, grad_w_gate, grad_w_up, grad_w_down)


def solution(mesh):
    placed = (
        P(("dp", "expert"), None),
        P(("dp", "expert"), None),
        P(("dp", "expert"), None),
        P("expert", "dp", None),
        P("expert", "dp", None),
        P("expert", None, "dp"),
        P(("dp", "expert"), None),
    )
    return jax.shard_map(
        shards,
        mesh=mesh,
        in_specs=placed,
        out_specs=(
            P(("dp", "expert"), None),
            P(("dp", "expert"), None),
            P(("dp", "expert"), None),
            P("expert", "dp", None),
            P("expert", "dp", None),
            P("expert", None, "dp"),
        ),
        check_vma=False,
    )
```

```python
import jax
import jax.numpy as jnp
from jax import lax
from jax.sharding import PartitionSpec as P


def route_slots(expert_ids, experts):
    flat_ids = expert_ids.reshape(-1)
    onehot = (flat_ids[:, None] == jnp.arange(experts, dtype=jnp.int32)[None, :]).astype(jnp.int32)
    before = jnp.cumsum(onehot, axis=0) - onehot
    slot_of = jnp.sum(before * onehot, axis=1)
    return flat_ids, slot_of


def contract_rows(left_op, right_op):
    return lax.dot_general(
        left_op, right_op, (((0,), (0,)), ((), ())), preferred_element_type=jnp.float32
    )


def contract_cols(left_op, right_op):
    return lax.dot_general(
        left_op, right_op, (((1,), (1,)), ((), ())), preferred_element_type=jnp.float32
    )


def shards(tokens, expert_ids, route_probs, w_gate, w_up, w_down, grad_out):
    senders = lax.axis_size("expert")
    tok_rows, model_width = tokens.shape
    top_count = expert_ids.shape[1]
    hidden_width = w_gate.shape[2]
    capacity = min(tok_rows, 4 * tok_rows * top_count // senders)
    total_rows = senders * capacity
    flat_ids, slot_of = route_slots(expert_ids, senders)

    packed = jnp.concatenate([w_gate[0], w_up[0], w_down[0].T], axis=1)
    whole = lax.all_gather(packed[None], "dp", axis=1, tiled=True)[0]
    gate_up = whole[:, : 2 * hidden_width]
    down_t = whole[:, 2 * hidden_width :]

    grad_wide = grad_out.astype(jnp.float32)
    scaled = (
        (route_probs.T[:, :, None] * grad_wide[None])
        .astype(jnp.bfloat16)
        .reshape(tok_rows * top_count, model_width)
    )
    base = flat_ids * (2 * capacity) + slot_of
    slots = jnp.arange(2 * total_rows, dtype=jnp.int32)[:, None]
    pairs = base.reshape(tok_rows, top_count)
    pick_tok = (slots == pairs[None, :, 0]) | (slots == pairs[None, :, 1])
    pick_grad = slots == (pairs.T.reshape(-1) + capacity)[None, :]
    chooser = jnp.concatenate([pick_tok, pick_grad], axis=1).astype(jnp.bfloat16)
    sources = jnp.concatenate([tokens, scaled], axis=0)
    outgoing = jnp.dot(chooser, sources, preferred_element_type=jnp.float32).astype(jnp.bfloat16)
    arrived = lax.all_to_all(
        outgoing.reshape(senders, 2 * capacity, model_width),
        "expert",
        split_axis=0,
        concat_axis=0,
        tiled=True,
    )
    arrived, whole = lax.optimization_barrier((arrived, whole))
    slot_rows = arrived[:, :capacity]
    grad_in = arrived[:, capacity:]
    on_width = (((2,), (0,)), ((), ()))
    on_rows = (((0, 1), (0, 1)), ((), ()))

    both_pre = lax.dot_general(
        slot_rows, gate_up, on_width, preferred_element_type=jnp.float32
    ).reshape(total_rows, 2 * hidden_width)
    gate_pre = both_pre[:, :hidden_width]
    up_pre = both_pre[:, hidden_width:]
    sigmoid_g = jax.nn.sigmoid(gate_pre)
    activated = gate_pre * sigmoid_g
    hidden = (activated * up_pre).astype(jnp.bfloat16)
    back_hidden = lax.dot_general(
        grad_in, down_t, on_width, preferred_element_type=jnp.float32
    ).reshape(total_rows, hidden_width)
    back_gate = (back_hidden * up_pre * sigmoid_g * (1.0 + gate_pre * (1.0 - sigmoid_g))).astype(
        jnp.bfloat16
    )
    back_up = (back_hidden * activated).astype(jnp.bfloat16)
    back_both = jnp.concatenate([back_gate, back_up], axis=1)

    grad_terms = jnp.concatenate(
        [
            lax.dot_general(
                slot_rows,
                back_both.reshape(senders, capacity, 2 * hidden_width),
                on_rows,
                preferred_element_type=jnp.float32,
            ).astype(jnp.bfloat16),
            lax.dot_general(
                grad_in,
                hidden.reshape(senders, capacity, hidden_width),
                on_rows,
                preferred_element_type=jnp.float32,
            ).astype(jnp.bfloat16),
        ],
        axis=1,
    )
    summed = lax.psum_scatter(grad_terms, "dp", scatter_dimension=0, tiled=True)

    expert_out = contract_cols(hidden, down_t).astype(jnp.bfloat16)
    back_rows = contract_cols(back_both, gate_up).astype(jnp.bfloat16)
    leaving = jnp.concatenate(
        [
            expert_out.reshape(senders, capacity, model_width),
            back_rows.reshape(senders, capacity, model_width),
        ],
        axis=1,
    )
    back_home = lax.all_to_all(leaving, "expert", split_axis=0, concat_axis=0, tiled=True)

    back_home, gate_sum, up_sum, down_sum = lax.optimization_barrier(
        (
            back_home,
            summed[:, :hidden_width],
            summed[:, hidden_width : 2 * hidden_width],
            summed[:, 2 * hidden_width :],
        )
    )
    own_place = (flat_ids * capacity + slot_of).reshape(tok_rows, top_count).T.reshape(-1)
    taker = (jnp.arange(total_rows, dtype=jnp.int32)[None, :] == own_place[:, None]).astype(
        jnp.bfloat16
    ).reshape(tok_rows * top_count, senders, capacity)
    picked, back_picked = (
        lax.dot_general(
            taker,
            back_home[:, half * capacity : (half + 1) * capacity],
            (((1, 2), (0, 1)), ((), ())),
            preferred_element_type=jnp.float32,
        ).reshape(top_count, tok_rows, model_width)
        for half in (0, 1)
    )
    probs_k = route_probs.T[:, :, None]
    mixed_out = jnp.sum(probs_k * picked, axis=0).astype(jnp.bfloat16)
    grad_probs = jnp.sum(grad_wide[None] * picked, axis=2).T
    grad_tokens = jnp.sum(back_picked.astype(jnp.float32), axis=0).astype(jnp.bfloat16)

    grad_w_gate = gate_sum[None]
    grad_w_up = up_sum[None]
    grad_w_down = down_sum.T[None]
    return (mixed_out, grad_tokens, grad_probs, grad_w_gate, grad_w_up, grad_w_down)


def solution(mesh):
    placed = (
        P(("dp", "expert"), None),
        P(("dp", "expert"), None),
        P(("dp", "expert"), None),
        P("expert", "dp", None),
        P("expert", "dp", None),
        P("expert", None, "dp"),
        P(("dp", "expert"), None),
    )
    return jax.shard_map(
        shards,
        mesh=mesh,
        in_specs=placed,
        out_specs=(
            P(("dp", "expert"), None),
            P(("dp", "expert"), None),
            P(("dp", "expert"), None),
            P("expert", "dp", None),
            P("expert", "dp", None),
            P("expert", None, "dp"),
        ),
        check_vma=False,
    )
```

```python
import jax
import jax.numpy as jnp
from jax import lax
from jax.sharding import PartitionSpec as P


def route_slots(expert_ids, experts):
    flat_ids = expert_ids.reshape(-1)
    onehot = (flat_ids[:, None] == jnp.arange(experts, dtype=jnp.int32)[None, :]).astype(jnp.int32)
    before = jnp.cumsum(onehot, axis=0) - onehot
    slot_of = jnp.sum(before * onehot, axis=1)
    return flat_ids, slot_of


def contract_rows(left_op, right_op):
    return lax.dot_general(
        left_op, right_op, (((0,), (0,)), ((), ())), preferred_element_type=jnp.float32
    )


def contract_cols(left_op, right_op):
    return lax.dot_general(
        left_op, right_op, (((1,), (1,)), ((), ())), preferred_element_type=jnp.float32
    )


def shards(tokens, expert_ids, route_probs, w_gate, w_up, w_down, grad_out):
    senders = lax.axis_size("expert")
    tok_rows, model_width = tokens.shape
    top_count = expert_ids.shape[1]
    hidden_width = w_gate.shape[2]
    capacity = min(tok_rows, 4 * tok_rows * top_count // senders)
    total_rows = senders * capacity
    flat_ids, slot_of = route_slots(expert_ids, senders)

    packed = jnp.concatenate([w_gate[0], w_up[0], w_down[0].T], axis=1)
    whole = lax.all_gather(packed[None], "dp", axis=1, tiled=True)[0]
    gate_up = whole[:, : 2 * hidden_width]
    down_t = whole[:, 2 * hidden_width :]

    grad_wide = grad_out.astype(jnp.float32)
    scaled = (
        (route_probs.T[:, :, None] * grad_wide[None])
        .astype(jnp.bfloat16)
        .reshape(tok_rows * top_count, model_width)
    )
    base = flat_ids * (2 * capacity) + slot_of
    slots = jnp.arange(2 * total_rows, dtype=jnp.int32)[:, None]
    pairs = base.reshape(tok_rows, top_count)
    pick_tok = (slots == pairs[None, :, 0]) | (slots == pairs[None, :, 1])
    pick_grad = slots == (pairs.T.reshape(-1) + capacity)[None, :]
    chooser = jnp.concatenate([pick_tok, pick_grad], axis=1).astype(jnp.bfloat16)
    sources = jnp.concatenate([tokens, scaled], axis=0)
    outgoing = jnp.dot(chooser, sources, preferred_element_type=jnp.float32).astype(jnp.bfloat16)
    arrived = lax.all_to_all(
        outgoing.reshape(senders, 2 * capacity, model_width),
        "expert",
        split_axis=0,
        concat_axis=0,
        tiled=True,
    )
    arrived, whole = lax.optimization_barrier((arrived, whole))
    slot_rows = arrived[:, :capacity].reshape(total_rows, model_width)
    grad_in = arrived[:, capacity:].reshape(total_rows, model_width)

    both_pre = jnp.dot(slot_rows, gate_up, preferred_element_type=jnp.float32)
    gate_pre = both_pre[:, :hidden_width]
    up_pre = both_pre[:, hidden_width:]
    sigmoid_g = jax.nn.sigmoid(gate_pre)
    activated = gate_pre * sigmoid_g
    hidden = (activated * up_pre).astype(jnp.bfloat16)
    back_hidden = jnp.dot(grad_in, down_t, preferred_element_type=jnp.float32)
    back_gate = (back_hidden * up_pre * sigmoid_g * (1.0 + gate_pre * (1.0 - sigmoid_g))).astype(
        jnp.bfloat16
    )
    back_up = (back_hidden * activated).astype(jnp.bfloat16)
    back_both = jnp.concatenate([back_gate, back_up], axis=1)

    grad_terms = jnp.concatenate(
        [
            contract_rows(grad_in, hidden).astype(jnp.bfloat16),
            contract_rows(slot_rows, back_both).astype(jnp.bfloat16),
        ],
        axis=1,
    )
    summed = lax.psum_scatter(grad_terms, "dp", scatter_dimension=0, tiled=True)

    expert_out = contract_cols(hidden, down_t).astype(jnp.bfloat16)
    back_rows = contract_cols(back_both, gate_up).astype(jnp.bfloat16)
    leaving = jnp.concatenate(
        [
            expert_out.reshape(senders, capacity, model_width),
            back_rows.reshape(senders, capacity, model_width),
        ],
        axis=1,
    )
    back_home = lax.all_to_all(leaving, "expert", split_axis=0, concat_axis=0, tiled=True)

    back_home, summed = lax.optimization_barrier((back_home, summed))
    own_place = (flat_ids * capacity + slot_of).reshape(tok_rows, top_count).T.reshape(-1)
    taker = (jnp.arange(total_rows, dtype=jnp.int32)[None, :] == own_place[:, None]).astype(
        jnp.bfloat16
    ).reshape(tok_rows * top_count, senders, capacity)
    picked, back_picked = (
        lax.dot_general(
            taker,
            back_home[:, half * capacity : (half + 1) * capacity],
            (((1, 2), (0, 1)), ((), ())),
            preferred_element_type=jnp.float32,
        ).reshape(top_count, tok_rows, model_width)
        for half in (0, 1)
    )
    probs_k = route_probs.T[:, :, None]
    mixed_out = jnp.sum(probs_k * picked, axis=0).astype(jnp.bfloat16)
    grad_probs = jnp.sum(grad_wide[None] * picked, axis=2).T
    grad_tokens = jnp.sum(back_picked.astype(jnp.float32), axis=0).astype(jnp.bfloat16)

    grad_w_down = summed[:, :hidden_width].T[None]
    grad_w_gate = summed[:, hidden_width : 2 * hidden_width][None]
    grad_w_up = summed[:, 2 * hidden_width :][None]
    return (mixed_out, grad_tokens, grad_probs, grad_w_gate, grad_w_up, grad_w_down)


def solution(mesh):
    placed = (
        P(("dp", "expert"), None),
        P(("dp", "expert"), None),
        P(("dp", "expert"), None),
        P("expert", "dp", None),
        P("expert", "dp", None),
        P("expert", None, "dp"),
        P(("dp", "expert"), None),
    )
    return jax.shard_map(
        shards,
        mesh=mesh,
        in_specs=placed,
        out_specs=(
            P(("dp", "expert"), None),
            P(("dp", "expert"), None),
            P(("dp", "expert"), None),
            P("expert", "dp", None),
            P("expert", "dp", None),
            P("expert", None, "dp"),
        ),
        check_vma=False,
    )
```
